512 devices in a mesh: box: 128 (over x, y, z_hi), slab: 4 (over z_lo, core).
Axes of the slice: x: 4, y: 8, z: 8 (z_hi: 4, z_lo: 2; z = z_hi * 2 + z_lo), core: 2. Of those that a mesh axis runs over, the one named last changes fastest.
Arguments:
- velocity: bfloat16 [128, 3, 8, 16, 64, 128], P('box', None, None, None, 'slab'), may hold values from -6 to 6
- field: float32 [128, 3, 8, 16, 64], P('box', None, None, None, 'slab'), may hold values from -6 to 6
- conductivity: float32 [128, 8, 16, 64], P('box', None, None, 'slab'), may hold values from 0.5 to 2
- wall_flags: int32 [128, 8, 16, 64], P('box', None, None, 'slab'), may hold values 0 or 1
- leaf_solution: bfloat16 [128, 4, 512, 2048], P('box', 'slab'), may hold values from -0.125 to 0.125
- leaf_dtn: float32 [128, 4, 512, 512], P('box', 'slab'), as said below
Outputs:
- interface_two: float32 [128, 4, 256, 128], P('box', 'slab')
- neumann_two: float32 [128, 4, 512, 128], P('box', 'slab')
The draws below stay inside these ranges and needn't reach their ends.
Inputs may be any that keep to these rules, and one draw needn't show every extreme that they name: `leaf_dtn`: every leaf map is symmetric positive definite.
All inputs are finite; a program needn't handle non-finite values. No bound on the sum of `wall_flags` on one device may be relied on, other than what follows from the above.
Results may differ from the reference program's by a relative error of at most 0.0029.
Values sent between devices are 32-bit elements; how exact they have to be, the bound alone decides.
No kernel may reach another device: no remote copies, remote signals or barrier semaphores. Data moves between devices by JAX's collectives and lax.ppermute only.
A program may use at most 64 MiB of HBM per device.

```python
import math
import jax
import jax.numpy as jnp
from jax import lax

LX = 8
LY = 16
R = 128
BOXES = 128
SLABS = 4
NZ = 64
FACE = 256
CELLS = 2048


DIAGONAL_SHIFT = 0.5


def draw_leaf_dtn(key, part):
    key_base = jax.random.fold_in(jax.random.fold_in(key, 7), 0)
    order = 2 * FACE
    shape = (BOXES, SLABS, order, order)
    factor = jax.random.normal(key_base, shape, jnp.float32)

    def gram(block):
        return jnp.einsum('sik,sjk->sij', block, block, precision=lax.Precision.HIGHEST)
    product = lax.map(gram, factor) * (1.0 / order)
    rows = jnp.arange(order, dtype=jnp.int32)
    identity = (rows[:, None] == rows[None, :]).astype(jnp.float32)
    result = product + DIAGONAL_SHIFT * identity
    return result


def with_ends(drawn, stream_key, smallest, top_value):
    index_at = [jax.random.randint(jax.random.fold_in(stream_key, axis), (), 0, length) for axis, length in enumerate(drawn.shape)]
    longest = drawn.shape.index(max(drawn.shape))
    next_to = index_at[:longest] + [(index_at[longest] + 1) % drawn.shape[longest]] + index_at[longest + 1:]
    return drawn.at[tuple(index_at)].set(smallest).at[tuple(next_to)].set(top_value)


def shard_levels(stream_key, dims, shards, low, largest):
    gain = 1.0
    for axis_at, parts in shards:
        steps = jax.random.uniform(jax.random.fold_in(jax.random.fold_in(stream_key, 6), axis_at), (parts,), jnp.float32, low / len(shards), largest / len(shards))
        gain = gain * jnp.repeat(jnp.exp(steps), dims[axis_at] // parts).reshape((-1,) + (1,) * (len(dims) - 1 - axis_at))
    return gain


def noise(stream_key, extent, deviation, bound, cuts=(), kind=jnp.bfloat16):
    gain = shard_levels(stream_key, extent, cuts, -0.22, 0.18) if cuts else 1.0
    entries = jax.random.normal(stream_key, extent, jnp.float32) * deviation * gain
    return jnp.minimum(jnp.maximum(entries, -bound), bound).astype(kind)


def setup_inputs(seed: int = 0) -> dict:
    seeds = jax.random.split(jax.random.key(seed), 7)
    return {
        "velocity": noise(seeds[0], (BOXES, 3, LX, LY, NZ, R), 1.0, 6.0, ((0, 128), (4, 4))),
        "field": noise(seeds[1], (BOXES, 3, LX, LY, NZ), 1.0, 6.0, ((0, 128), (4, 4)), jnp.float32),
        "conductivity": jnp.clip(jnp.exp(math.log(2.0) - 1.3862944 * jax.random.uniform(seeds[2], (BOXES, LX, LY, NZ), jnp.float32) ** shard_levels(seeds[2], (BOXES, LX, LY, NZ), ((0, 128), (3, 4)), -0.2, 0.2)), 0.5, 2.0),
        "wall_flags": with_ends((jax.random.randint(seeds[3], (BOXES, LX, LY, NZ), 0, 4) < 1).astype(jnp.int32), jax.random.fold_in(seeds[3], 1), 0, 1),
        "leaf_solution": noise(seeds[4], (BOXES, SLABS, 2 * FACE, CELLS), CELLS ** -0.5, 0.125, ((0, 128), (1, 4))),
        "leaf_dtn": draw_leaf_dtn(jax.random.fold_in(seeds[6], 71), 0),
    }


WALL_RATIO = 8.0
HIGHEST = lax.Precision.HIGHEST

def currents(velocity, field, conductivity, wall_flags):
    sigma = conductivity * jnp.where(wall_flags == 1, WALL_RATIO, 1.0).astype(conductivity.dtype)
    speed = velocity.astype(jnp.float32)
    magnet = field[..., None]
    weight = sigma[..., None]
    elec_x = speed[1] * magnet[2] - speed[2] * magnet[1]
    elec_y = speed[2] * magnet[0] - speed[0] * magnet[2]
    elec_z = speed[0] * magnet[1] - speed[1] * magnet[0]
    return (weight * elec_x, weight * elec_y, weight * elec_z)

def divergence(flow_x, flow_y, padded_z):
    padded_x = jnp.pad(flow_x, ((1, 1), (0, 0), (0, 0), (0, 0)))
    padded_y = jnp.pad(flow_y, ((0, 0), (1, 1), (0, 0), (0, 0)))
    return 0.5 * (padded_x[2:] - padded_x[:-2] + (padded_y[:, 2:] - padded_y[:, :-2]) + (padded_z[:, :, 2:] - padded_z[:, :, :-2]))

def merge(left_map, left_data, right_map, right_data, need_map):
    width = left_map.shape[0] // 2
    schur = left_map[width:, width:] + right_map[:width, :width]
    coupling = jnp.concatenate([left_map[width:, :width], right_map[:width, width:]], axis=1)
    stacked = jnp.concatenate([coupling, left_data[width:] + right_data[:width]], axis=1)
    solved = jnp.linalg.solve(schur, stacked)
    interface = -solved[:, 2 * width:]
    outward = jnp.concatenate([left_map[:width, width:], right_map[width:, :width]], axis=0)
    parent_data = jnp.concatenate([left_data[:width], right_data[width:]], axis=0) + jnp.dot(outward, interface, precision=HIGHEST)
    parent_map = None
    if need_map:
        zeros = jnp.zeros((width, width), left_map.dtype)
        base = jnp.concatenate([jnp.concatenate([left_map[:width, :width], zeros], axis=1), jnp.concatenate([zeros, right_map[width:, width:]], axis=1)], axis=0)
        parent_map = base - jnp.dot(outward, solved[:, :2 * width], precision=HIGHEST)
    return (parent_map, parent_data, interface)

def level(maps, datas, need_map):
    count = maps.shape[0]
    paired_maps = maps.reshape((count // 2, 2) + maps.shape[1:])
    paired_data = datas.reshape((count // 2, 2) + datas.shape[1:])

    def one_pair(items):
        pair_maps, pair_data = items
        return jax.vmap(lambda lmap, ldat, rmap, rdat: merge(lmap, ldat, rmap, rdat, need_map))(pair_maps[0], pair_data[0], pair_maps[1], pair_data[1])
    return lax.map(one_pair, (paired_maps, paired_data))

def reference(velocity, field, conductivity, wall_flags, leaf_solution, leaf_dtn):
    slabs = leaf_solution.shape[1]
    depth = velocity.shape[4] // slabs

    def per_box(items):
        speed, magnet, conduct, flags, solution = items
        flow_x, flow_y, flow_z = currents(speed, magnet, conduct, flags)
        padded_z = jnp.pad(flow_z, ((0, 0), (0, 0), (1, 1), (0, 0)))
        source = divergence(flow_x, flow_y, padded_z).astype(jnp.bfloat16)
        sizex, sizey, total, snaps = source.shape
        blocks = source.reshape(sizex, sizey, slabs, depth, snaps).transpose(2, 0, 1, 3, 4).reshape(slabs, sizex * sizey * depth, snaps)
        return jnp.einsum('sfc,scr->sfr', solution.astype(jnp.float32), blocks.astype(jnp.float32))
    neumann_zero = lax.map(per_box, (velocity, field, conductivity, wall_flags, leaf_solution))
    map_one, neumann_one, interface_one = level(leaf_dtn, neumann_zero, True)
    unused, neumann_two, interface_two = level(map_one, neumann_one, False)
    return (jnp.repeat(interface_two, 4, axis=0), jnp.repeat(neumann_two, 4, axis=0))
```

```python
import jax
import jax.numpy as jnp
from jax import lax
from jax.sharding import PartitionSpec as P

WALL_RATIO = 8.0
HIGHEST = lax.Precision.HIGHEST


def padded_2(block, sides, width):
    for axis, dim in sides:
        count = lax.axis_size(axis)
        forward = [(i, i + 1) for i in range(count - 1)]
        backward = [(target, source) for source, target in forward]
        low = lax.ppermute(
            lax.slice_in_dim(block, block.shape[dim] - width, None, axis=dim), axis, forward
        )
        high = lax.ppermute(lax.slice_in_dim(block, 0, width, axis=dim), axis, backward)
        block = jnp.concatenate([low, block, high], axis=dim)
    return block


def currents(velocity, field, conductivity, wall_flags):
    sigma = conductivity * jnp.where(wall_flags == 1, WALL_RATIO, 1.0).astype(conductivity.dtype)
    speed = velocity.astype(jnp.float32)
    magnet = field[..., None]
    weight = sigma[..., None]
    elec_x = speed[1] * magnet[2] - speed[2] * magnet[1]
    elec_y = speed[2] * magnet[0] - speed[0] * magnet[2]
    elec_z = speed[0] * magnet[1] - speed[1] * magnet[0]
    return (weight * elec_x, weight * elec_y, weight * elec_z)


def divergence(flow_x, flow_y, padded_z):
    padded_x = jnp.pad(flow_x, ((1, 1), (0, 0), (0, 0), (0, 0)))
    padded_y = jnp.pad(flow_y, ((0, 0), (1, 1), (0, 0), (0, 0)))
    return 0.5 * (
        padded_x[2:]
        - padded_x[:-2]
        + (padded_y[:, 2:] - padded_y[:, :-2])
        + (padded_z[:, :, 2:] - padded_z[:, :, :-2])
    )


def schur_solve(schur, stacked):
    factor = jnp.linalg.cholesky(schur)
    return jax.scipy.linalg.cho_solve((factor, True), stacked)


def dot(a, b):
    return jnp.dot(a, b, precision=HIGHEST)


def group_route(count, pairs):
    route = []
    for base in range(0, count, 4):
        route += [(base + s, base + t) for s, t in pairs]
    return route


def take(block, start, size, axis):
    return lax.dynamic_slice_in_dim(block, start, size, axis=axis)


def on_device(velocity, field, conductivity, wall_flags, leaf_solution, leaf_dtn):
    count = lax.axis_size("box")
    dtn_map = leaf_dtn[0, 0]
    width = dtn_map.shape[0] // 2
    place = lax.axis_index("box") % 4
    odd = place % 2
    near = (1 - odd) * width
    far = odd * width

    inward = group_route(count, [(0, 1), (3, 2)])
    sent_map = lax.ppermute(take(dtn_map, near, width, 1), "box", inward)

    flow_x, flow_y, flow_z = currents(velocity[0], field[0], conductivity[0], wall_flags[0])
    solution_map = leaf_solution[0, 0]
    sizex, sizey, depth, snaps = flow_x.shape
    cell_count = sizex * sizey * depth
    padded = padded_2(flow_z, (("slab", 2),), 1)
    source = divergence(flow_x, flow_y, padded).astype(jnp.bfloat16)
    neumann = jnp.dot(
        solution_map, source.reshape(cell_count, snaps), preferred_element_type=jnp.float32
    )
    sent_data = lax.ppermute(neumann, "box", inward)

    own_nn = take(take(dtn_map, near, width, 0), near, width, 1)
    own_nf = take(take(dtn_map, near, width, 0), far, width, 1)
    own_fn = take(take(dtn_map, far, width, 0), near, width, 1)
    own_ff = take(take(dtn_map, far, width, 0), far, width, 1)
    part_nn = take(sent_map, far, width, 0)
    part_fn = take(sent_map, near, width, 0)
    schur = own_nn + part_nn
    rhs = take(neumann, near, width, 0) + take(sent_data, far, width, 0)
    solved = schur_solve(schur, jnp.concatenate([own_nf, rhs], axis=1))
    solved_map = solved[:, :width]
    first_face = -solved[:, width:]
    far_map = own_ff - dot(own_fn, solved_map)
    cross_map = -dot(part_fn, solved_map)
    far_data = take(neumann, far, width, 0) + dot(own_fn, first_face)
    part_data = take(sent_data, near, width, 0) + dot(part_fn, first_face)

    swap = group_route(count, [(1, 2), (2, 1)])
    other = lax.ppermute(jnp.concatenate([far_map, far_data], axis=1), "box", swap)
    schur_two = far_map + other[:, :width]
    rhs_two = far_data + other[:, width:]
    interface_two = -schur_solve(schur_two, rhs_two)
    half = part_data + dot(cross_map, interface_two)

    outer = lax.ppermute(
        jnp.concatenate([interface_two, half], axis=1), "box", group_route(count, [(1, 0), (2, 3)])
    )
    inner = lax.ppermute(half, "box", swap)
    across = lax.ppermute(half, "box", group_route(count, [(1, 3), (2, 0)]))
    snaps_two = interface_two.shape[1]
    is_inner = (place == 1) | (place == 2)
    interface_out = jnp.where(is_inner, interface_two, outer[:, :snaps_two])
    outer_half = outer[:, snaps_two:]
    top = jnp.where(
        place == 0, outer_half, jnp.where(place == 1, half, jnp.where(place == 2, inner, across))
    )
    bottom = jnp.where(
        place == 0, across, jnp.where(place == 1, inner, jnp.where(place == 2, half, outer_half))
    )
    neumann_two = jnp.concatenate([top, bottom], axis=0)
    return (interface_out[None, None], neumann_two[None, None])


def solution(mesh):
    return jax.shard_map(
        on_device,
        mesh=mesh,
        in_specs=(
            P("box", None, None, None, "slab", None),
            P("box", None, None, None, "slab"),
            P("box", None, None, "slab"),
            P("box", None, None, "slab"),
            P("box", "slab", None, None),
            P("box", "slab", None, None),
        ),
        out_specs=(P("box", "slab", None, None), P("box", "slab", None, None)),
        check_vma=False,
    )
```

```python
import jax
import jax.numpy as jnp
from jax import lax
from jax.sharding import PartitionSpec as P
from jax.experimental import pallas as pl

WALL_RATIO = 8.0
HIGHEST = lax.Precision.HIGHEST


def padded_2(block, sides, width):
    for axis, dim in sides:
        count = lax.axis_size(axis)
        forward = [(i, i + 1) for i in range(count - 1)]
        backward = [(target, source) for source, target in forward]
        low = lax.ppermute(
            lax.slice_in_dim(block, block.shape[dim] - width, None, axis=dim), axis, forward
        )
        high = lax.ppermute(lax.slice_in_dim(block, 0, width, axis=dim), axis, backward)
        block = jnp.concatenate([low, block, high], axis=dim)
    return block


def currents(velocity, field, conductivity, wall_flags):
    sigma = conductivity * jnp.where(wall_flags == 1, WALL_RATIO, 1.0).astype(conductivity.dtype)
    speed = velocity.astype(jnp.float32)
    magnet = field[..., None]
    weight = sigma[..., None]
    elec_x = speed[1] * magnet[2] - speed[2] * magnet[1]
    elec_y = speed[2] * magnet[0] - speed[0] * magnet[2]
    elec_z = speed[0] * magnet[1] - speed[1] * magnet[0]
    return (weight * elec_x, weight * elec_y, weight * elec_z)


def divergence(flow_x, flow_y, padded_z):
    padded_x = jnp.pad(flow_x, ((1, 1), (0, 0), (0, 0), (0, 0)))
    padded_y = jnp.pad(flow_y, ((0, 0), (1, 1), (0, 0), (0, 0)))
    return 0.5 * (
        padded_x[2:]
        - padded_x[:-2]
        + (padded_y[:, 2:] - padded_y[:, :-2])
        + (padded_z[:, :, 2:] - padded_z[:, :, :-2])
    )


def sweep_kernel(a_ref, o_ref):
    n = a_ref.shape[0]
    o_ref[...] = a_ref[...]
    lane = lax.broadcasted_iota(jnp.int32, (1, n), 1)
    sub = lax.broadcasted_iota(jnp.int32, (n, 1), 0)

    def body(k, carry):
        whole = o_ref[...]
        row = o_ref[pl.ds(k, 1), :]
        pick = lane == k
        pivot = jnp.sum(jnp.where(pick, row, 0.0), axis=1, keepdims=True)
        scale = 1.0 / pivot
        lead = row * scale - jnp.where(pick, scale, 0.0)
        column = jnp.sum(jnp.where(pick, whole, 0.0), axis=1, keepdims=True)
        column = column - jnp.where(sub == k, 1.0, 0.0)
        o_ref[...] = whole - column * lead
        o_ref[pl.ds(k, 1), :] = lead - jnp.where(pick, 1.0, 0.0)
        return carry

    lax.fori_loop(0, n, body, 0)


def neg_inverse(block):
    n = block.shape[0]
    return pl.pallas_call(
        sweep_kernel,
        out_shape=jax.ShapeDtypeStruct(block.shape, block.dtype),
        cost_estimate=pl.CostEstimate(
            flops=2 * n * n * n, bytes_accessed=8 * n * n, transcendentals=0
        ),
    )(block)


def schur_solve(schur, stacked):
    h = schur.shape[0] // 2
    upper, right = schur[:h, :h], schur[:h, h:]
    left, lower = schur[h:, :h], schur[h:, h:]
    upper_inv = -neg_inverse(upper)
    reach = dot(upper_inv, right)
    lower_inv = -neg_inverse(lower - dot(left, reach))
    first = dot(upper_inv, stacked[:h])
    second = dot(lower_inv, stacked[h:] - dot(left, first))
    return jnp.concatenate([first - dot(reach, second), second], axis=0)


def dot(a, b):
    return jnp.dot(a, b, precision=HIGHEST)


def group_route(count, pairs):
    route = []
    for base in range(0, count, 4):
        route += [(base + s, base + t) for s, t in pairs]
    return route


def take(block, start, size, axis):
    return lax.dynamic_slice_in_dim(block, start, size, axis=axis)


def on_device(velocity, field, conductivity, wall_flags, leaf_solution, leaf_dtn):
    count = lax.axis_size("box")
    dtn_map = leaf_dtn[0, 0]
    width = dtn_map.shape[0] // 2
    place = lax.axis_index("box") % 4
    odd = place % 2
    near = (1 - odd) * width
    far = odd * width

    inward = group_route(count, [(0, 1), (3, 2)])
    sent_map = lax.ppermute(take(dtn_map, near, width, 1), "box", inward)

    flow_x, flow_y, flow_z = currents(velocity[0], field[0], conductivity[0], wall_flags[0])
    solution_map = leaf_solution[0, 0]
    sizex, sizey, depth, snaps = flow_x.shape
    cell_count = sizex * sizey * depth
    padded = padded_2(flow_z, (("slab", 2),), 1)
    source = divergence(flow_x, flow_y, padded).astype(jnp.bfloat16)
    neumann = jnp.dot(
        solution_map, source.reshape(cell_count, snaps), preferred_element_type=jnp.float32
    )
    sent_data = lax.ppermute(neumann, "box", inward)

    own_nn = take(take(dtn_map, near, width, 0), near, width, 1)
    own_nf = take(take(dtn_map, near, width, 0), far, width, 1)
    own_fn = take(take(dtn_map, far, width, 0), near, width, 1)
    own_ff = take(take(dtn_map, far, width, 0), far, width, 1)
    part_nn = take(sent_map, far, width, 0)
    part_fn = take(sent_map, near, width, 0)
    schur = own_nn + part_nn
    rhs = take(neumann, near, width, 0) + take(sent_data, far, width, 0)
    solved = schur_solve(schur, jnp.concatenate([own_nf, rhs], axis=1))
    solved_map = solved[:, :width]
    first_face = -solved[:, width:]
    far_map = own_ff - dot(own_fn, solved_map)
    cross_map = -dot(part_fn, solved_map)
    far_data = take(neumann, far, width, 0) + dot(own_fn, first_face)
    part_data = take(sent_data, near, width, 0) + dot(part_fn, first_face)

    swap = group_route(count, [(1, 2), (2, 1)])
    other = lax.ppermute(jnp.concatenate([far_map, far_data], axis=1), "box", swap)
    schur_two = far_map + other[:, :width]
    rhs_two = far_data + other[:, width:]
    interface_two = -schur_solve(schur_two, rhs_two)
    half = part_data + dot(cross_map, interface_two)

    outer = lax.ppermute(
        jnp.concatenate([interface_two, half], axis=1), "box", group_route(count, [(1, 0), (2, 3)])
    )
    inner = lax.ppermute(half, "box", swap)
    across = lax.ppermute(half, "box", group_route(count, [(1, 3), (2, 0)]))
    snaps_two = interface_two.shape[1]
    is_inner = (place == 1) | (place == 2)
    interface_out = jnp.where(is_inner, interface_two, outer[:, :snaps_two])
    outer_half = outer[:, snaps_two:]
    top = jnp.where(
        place == 0, outer_half, jnp.where(place == 1, half, jnp.where(place == 2, inner, across))
    )
    bottom = jnp.where(
        place == 0, across, jnp.where(place == 1, inner, jnp.where(place == 2, half, outer_half))
    )
    neumann_two = jnp.concatenate([top, bottom], axis=0)
    return (interface_out[None, None], neumann_two[None, None])


def solution(mesh):
    return jax.shard_map(
        on_device,
        mesh=mesh,
        in_specs=(
            P("box", None, None, None, "slab", None),
            P("box", None, None, None, "slab"),
            P("box", None, None, "slab"),
            P("box", None, None, "slab"),
            P("box", "slab", None, None),
            P("box", "slab", None, None),
        ),
        out_specs=(P("box", "slab", None, None), P("box", "slab", None, None)),
        check_vma=False,
    )
```

```python
import jax
import jax.numpy as jnp
from jax import lax
from jax.sharding import PartitionSpec as P
from jax.experimental import pallas as pl

WALL_RATIO = 8.0
HIGHEST = lax.Precision.HIGHEST


def padded_2(block, sides, width):
    for axis, dim in sides:
        count = lax.axis_size(axis)
        forward = [(i, i + 1) for i in range(count - 1)]
        backward = [(target, source) for source, target in forward]
        low = lax.ppermute(
            lax.slice_in_dim(block, block.shape[dim] - width, None, axis=dim), axis, forward
        )
        high = lax.ppermute(lax.slice_in_dim(block, 0, width, axis=dim), axis, backward)
        block = jnp.concatenate([low, block, high], axis=dim)
    return block


def currents(velocity, field, conductivity, wall_flags):
    sigma = conductivity * jnp.where(wall_flags == 1, WALL_RATIO, 1.0).astype(conductivity.dtype)
    speed = velocity.astype(jnp.float32)
    magnet = field[..., None]
    weight = sigma[..., None]
    elec_x = speed[1] * magnet[2] - speed[2] * magnet[1]
    elec_y = speed[2] * magnet[0] - speed[0] * magnet[2]
    elec_z = speed[0] * magnet[1] - speed[1] * magnet[0]
    return (weight * elec_x, weight * elec_y, weight * elec_z)


def divergence(flow_x, flow_y, padded_z):
    padded_x = jnp.pad(flow_x, ((1, 1), (0, 0), (0, 0), (0, 0)))
    padded_y = jnp.pad(flow_y, ((0, 0), (1, 1), (0, 0), (0, 0)))
    return 0.5 * (
        padded_x[2:]
        - padded_x[:-2]
        + (padded_y[:, 2:] - padded_y[:, :-2])
        + (padded_z[:, :, 2:] - padded_z[:, :, :-2])
    )


def sweep_kernel(a_ref, o_ref):
    n = a_ref.shape[0]
    o_ref[...] = a_ref[...]
    lane = lax.broadcasted_iota(jnp.int32, (1, n), 1)
    sub = lax.broadcasted_iota(jnp.int32, (n, 1), 0)

    def body(k, carry):
        whole = o_ref[...]
        row = o_ref[pl.ds(k, 1), :]
        pick = lane == k
        pivot = jnp.sum(jnp.where(pick, row, 0.0), axis=1, keepdims=True)
        scale = 1.0 / pivot
        lead = row * scale - jnp.where(pick, scale, 0.0)
        column = jnp.sum(jnp.where(pick, whole, 0.0), axis=1, keepdims=True)
        column = column - jnp.where(sub == k, 1.0, 0.0)
        o_ref[...] = whole - column * lead
        o_ref[pl.ds(k, 1), :] = lead - jnp.where(pick, 1.0, 0.0)
        return carry

    lax.fori_loop(0, n, body, 0)


def neg_inverse(block):
    n = block.shape[0]
    return pl.pallas_call(
        sweep_kernel,
        out_shape=jax.ShapeDtypeStruct(block.shape, block.dtype),
        cost_estimate=pl.CostEstimate(
            flops=8000 * n * n * n, bytes_accessed=8 * n * n, transcendentals=0
        ),
    )(block)


def inverse_parts(schur):
    h = schur.shape[0] // 2
    upper_inv = -neg_inverse(schur[:h, :h])
    reach = dot(upper_inv, schur[:h, h:])
    left = schur[h:, :h]
    lower_inv = -neg_inverse(schur[h:, h:] - dot(left, reach))
    return (upper_inv, reach, left, lower_inv)


def apply_inverse(parts, stacked):
    upper_inv, reach, left, lower_inv = parts
    h = upper_inv.shape[0]
    first = dot(upper_inv, stacked[:h])
    second = dot(lower_inv, stacked[h:] - dot(left, first))
    return jnp.concatenate([first - dot(reach, second), second], axis=0)


def dot(a, b):
    return jnp.dot(a, b, precision=HIGHEST)


def group_route(count, pairs):
    route = []
    for base in range(0, count, 4):
        route += [(base + s, base + t) for s, t in pairs]
    return route


def take(block, start, size, axis):
    return lax.dynamic_slice_in_dim(block, start, size, axis=axis)


def upward(velocity, field, conductivity, wall_flags, leaf_solution, leaf_dtn):
    count = lax.axis_size("box")
    dtn_map = leaf_dtn[0, 0]
    width = dtn_map.shape[0] // 2
    place = lax.axis_index("box") % 4
    odd = place % 2
    near = (1 - odd) * width
    far = odd * width

    own_nn = take(take(dtn_map, near, width, 0), near, width, 1)
    own_nf = take(take(dtn_map, near, width, 0), far, width, 1)
    own_fn = take(take(dtn_map, far, width, 0), near, width, 1)
    own_ff = take(take(dtn_map, far, width, 0), far, width, 1)

    inward = group_route(count, [(0, 1), (3, 2)])
    part_nn = lax.ppermute(own_nn, "box", inward)

    flow_x, flow_y, flow_z = currents(velocity[0], field[0], conductivity[0], wall_flags[0])
    solution_map = leaf_solution[0, 0]
    sizex, sizey, depth, snaps = flow_x.shape
    cell_count = sizex * sizey * depth
    padded = padded_2(flow_z, (("slab", 2),), 1)
    source = divergence(flow_x, flow_y, padded).astype(jnp.bfloat16)
    neumann = jnp.dot(
        solution_map, source.reshape(cell_count, snaps), preferred_element_type=jnp.float32
    )
    own_near = take(neumann, near, width, 0)
    own_far = take(neumann, far, width, 0)
    sent = lax.ppermute(jnp.concatenate([own_fn, own_near, own_far], axis=1), "box", inward)

    parts = inverse_parts(own_nn + part_nn)
    solved_map = apply_inverse(parts, own_nf)
    far_map = own_ff - dot(own_fn, solved_map)

    swap = group_route(count, [(1, 2), (2, 1)])
    other_map = lax.ppermute(far_map, "box", swap)
    parts_two = inverse_parts(far_map + other_map)

    part_fn = sent[:, :width]
    snaps = neumann.shape[1]
    part_near = sent[:, width : width + snaps]
    part_far = sent[:, width + snaps :]
    first_face = -apply_inverse(parts, own_near + part_near)
    cross_map = -dot(part_fn, solved_map)
    far_data = own_far + dot(own_fn, first_face)
    part_data = part_far + dot(part_fn, first_face)
    other_data = lax.ppermute(far_data, "box", swap)
    interface_two = -apply_inverse(parts_two, far_data + other_data)
    half = part_data + dot(cross_map, interface_two)

    outer = lax.ppermute(
        jnp.concatenate([interface_two, half], axis=1), "box", group_route(count, [(1, 0), (2, 3)])
    )
    inner = lax.ppermute(half, "box", swap)
    across = lax.ppermute(half, "box", group_route(count, [(1, 3), (2, 0)]))
    snaps_two = interface_two.shape[1]
    is_inner = (place == 1) | (place == 2)
    interface_out = jnp.where(is_inner, interface_two, outer[:, :snaps_two])
    outer_half = outer[:, snaps_two:]
    top = jnp.where(
        place == 0, outer_half, jnp.where(place == 1, half, jnp.where(place == 2, inner, across))
    )
    bottom = jnp.where(
        place == 0, across, jnp.where(place == 1, inner, jnp.where(place == 2, half, outer_half))
    )
    neumann_two = jnp.concatenate([top, bottom], axis=0)
    return (interface_out[None, None], neumann_two[None, None])


def solution(mesh):
    return jax.shard_map(
        upward,
        mesh=mesh,
        in_specs=(
            P("box", None, None, None, "slab", None),
            P("box", None, None, None, "slab"),
            P("box", None, None, "slab"),
            P("box", None, None, "slab"),
            P("box", "slab", None, None),
            P("box", "slab", None, None),
        ),
        out_specs=(P("box", "slab", None, None), P("box", "slab", None, None)),
        check_vma=False,
    )
```

```python
import jax
import jax.numpy as jnp
from jax import lax
from jax.sharding import PartitionSpec as P
from jax.experimental import pallas as pl

WALL_RATIO = 8.0
HIGH = lax.Precision.HIGH


def padded_2(block, sides, width):
    for axis, dim in sides:
        count = lax.axis_size(axis)
        forward = [(i, i + 1) for i in range(count - 1)]
        backward = [(target, source) for source, target in forward]
        low = lax.ppermute(
            lax.slice_in_dim(block, block.shape[dim] - width, None, axis=dim), axis, forward
        )
        high = lax.ppermute(lax.slice_in_dim(block, 0, width, axis=dim), axis, backward)
        block = jnp.concatenate([low, block, high], axis=dim)
    return block


def currents(velocity, field, conductivity, wall_flags):
    sigma = conductivity * jnp.where(wall_flags == 1, WALL_RATIO, 1.0).astype(conductivity.dtype)
    speed = velocity.astype(jnp.float32)
    magnet = field[..., None]
    weight = sigma[..., None]
    elec_x = speed[1] * magnet[2] - speed[2] * magnet[1]
    elec_y = speed[2] * magnet[0] - speed[0] * magnet[2]
    elec_z = speed[0] * magnet[1] - speed[1] * magnet[0]
    return (weight * elec_x, weight * elec_y, weight * elec_z)


def divergence(flow_x, flow_y, padded_z):
    padded_x = jnp.pad(flow_x, ((1, 1), (0, 0), (0, 0), (0, 0)))
    padded_y = jnp.pad(flow_y, ((0, 0), (1, 1), (0, 0), (0, 0)))
    return 0.5 * (
        padded_x[2:]
        - padded_x[:-2]
        + (padded_y[:, 2:] - padded_y[:, :-2])
        + (padded_z[:, :, 2:] - padded_z[:, :, :-2])
    )


def sweep_kernel(a_ref, o_ref):
    n = a_ref.shape[0]
    o_ref[...] = a_ref[...]
    lane = lax.broadcasted_iota(jnp.int32, (1, n), 1)
    sub = lax.broadcasted_iota(jnp.int32, (n, 1), 0)

    def body(k, carry):
        whole = o_ref[...]
        row = o_ref[pl.ds(k, 1), :]
        pick = lane == k
        pivot = jnp.sum(jnp.where(pick, row, 0.0), axis=1, keepdims=True)
        scale = 1.0 / pivot
        lead = row * scale - jnp.where(pick, scale, 0.0)
        column = jnp.sum(jnp.where(pick, whole, 0.0), axis=1, keepdims=True)
        column = column - jnp.where(sub == k, 1.0, 0.0)
        o_ref[...] = whole - column * lead
        o_ref[pl.ds(k, 1), :] = lead - jnp.where(pick, 1.0, 0.0)
        return carry

    lax.fori_loop(0, n, body, 0)


def neg_inverse(block):
    n = block.shape[0]
    return pl.pallas_call(
        sweep_kernel,
        out_shape=jax.ShapeDtypeStruct(block.shape, block.dtype),
        cost_estimate=pl.CostEstimate(
            flops=8000 * n * n * n, bytes_accessed=8 * n * n, transcendentals=0
        ),
    )(block)


def inverse_parts(schur):
    h = schur.shape[0] // 2
    upper_inv = -neg_inverse(schur[:h, :h])
    reach = dot(upper_inv, schur[:h, h:])
    left = schur[h:, :h]
    lower_inv = -neg_inverse(schur[h:, h:] - dot(left, reach))
    return (upper_inv, reach, left, lower_inv)


def apply_inverse(parts, stacked):
    upper_inv, reach, left, lower_inv = parts
    h = upper_inv.shape[0]
    first = dot(upper_inv, stacked[:h])
    second = dot(lower_inv, stacked[h:] - dot(left, first))
    return jnp.concatenate([first - dot(reach, second), second], axis=0)


def dot(a, b):
    return jnp.dot(a, b, precision=HIGH)


def pack_symmetric(block):
    h = block.shape[0] // 2
    rows = lax.broadcasted_iota(jnp.int32, (h, h), 0)
    cols = lax.broadcasted_iota(jnp.int32, (h, h), 1)
    corner = jnp.where(rows >= cols, block[:h, :h], block[h:, h:])
    diagonal = jnp.sum(jnp.where(rows == cols, block[h:, h:], 0.0), axis=0, keepdims=True)
    fill = jnp.zeros((7, h), block.dtype)
    return jnp.concatenate([block[h:, :h], corner, diagonal, fill], axis=0)


def unpack_symmetric(packed):
    h = packed.shape[1]
    rows = lax.broadcasted_iota(jnp.int32, (h, h), 0)
    cols = lax.broadcasted_iota(jnp.int32, (h, h), 1)
    lower_left = packed[:h]
    corner = packed[h : 2 * h]
    diagonal = packed[2 * h : 2 * h + 1]
    upper = jnp.where(rows >= cols, corner, corner.T)
    lower = jnp.where(rows == cols, diagonal, jnp.where(rows < cols, corner, corner.T))
    return jnp.concatenate(
        [
            jnp.concatenate([upper, lower_left.T], axis=1),
            jnp.concatenate([lower_left, lower], axis=1),
        ],
        axis=0,
    )


def group_route(count, pairs):
    route = []
    for base in range(0, count, 4):
        route += [(base + s, base + t) for s, t in pairs]
    return route


def take(block, start, size, axis):
    return lax.dynamic_slice_in_dim(block, start, size, axis=axis)


def upward(velocity, field, conductivity, wall_flags, leaf_solution, leaf_dtn):
    count = lax.axis_size("box")
    dtn_map = leaf_dtn[0, 0]
    width = dtn_map.shape[0] // 2
    place = lax.axis_index("box") % 4
    odd = place % 2
    near = (1 - odd) * width
    far = odd * width

    own_nn = take(take(dtn_map, near, width, 0), near, width, 1)
    own_nf = take(take(dtn_map, near, width, 0), far, width, 1)
    own_fn = take(take(dtn_map, far, width, 0), near, width, 1)
    own_ff = take(take(dtn_map, far, width, 0), far, width, 1)

    inward = group_route(count, [(0, 1), (3, 2)])
    part_nn = unpack_symmetric(lax.ppermute(pack_symmetric(own_nn), "box", inward))

    flow_x, flow_y, flow_z = currents(velocity[0], field[0], conductivity[0], wall_flags[0])
    solution_map = leaf_solution[0, 0]
    sizex, sizey, depth, snaps = flow_x.shape
    cell_count = sizex * sizey * depth
    padded = padded_2(flow_z, (("slab", 2),), 1)
    source = divergence(flow_x, flow_y, padded).astype(jnp.bfloat16)
    neumann = jnp.dot(
        solution_map, source.reshape(cell_count, snaps), preferred_element_type=jnp.float32
    )
    own_near = take(neumann, near, width, 0)
    own_far = take(neumann, far, width, 0)
    sent = lax.ppermute(jnp.concatenate([own_fn, own_near, own_far], axis=1), "box", inward)

    parts = inverse_parts(own_nn + part_nn)
    solved_map = apply_inverse(parts, own_nf)
    far_map = own_ff - dot(own_fn, solved_map)

    swap = group_route(count, [(1, 2), (2, 1)])
    packed_far = pack_symmetric(far_map)
    other_map = unpack_symmetric(lax.ppermute(packed_far, "box", swap))
    parts_two = inverse_parts(unpack_symmetric(packed_far) + other_map)

    part_fn = sent[:, :width]
    snaps = neumann.shape[1]
    part_near = sent[:, width : width + snaps]
    part_far = sent[:, width + snaps :]
    first_face = -apply_inverse(parts, own_near + part_near)
    cross_map = -dot(part_fn, solved_map)
    far_data = own_far + dot(own_fn, first_face)
    part_data = part_far + dot(part_fn, first_face)
    other_data = lax.ppermute(far_data, "box", swap)
    interface_two = -apply_inverse(parts_two, far_data + other_data)
    half = part_data + dot(cross_map, interface_two)

    outer = lax.ppermute(
        jnp.concatenate([interface_two, half], axis=1), "box", group_route(count, [(1, 0), (2, 3)])
    )
    inner = lax.ppermute(half, "box", swap)
    across = lax.ppermute(half, "box", group_route(count, [(1, 3), (2, 0)]))
    snaps_two = interface_two.shape[1]
    is_inner = (place == 1) | (place == 2)
    interface_out = jnp.where(is_inner, interface_two, outer[:, :snaps_two])
    outer_half = outer[:, snaps_two:]
    top = jnp.where(
        place == 0, outer_half, jnp.where(place == 1, half, jnp.where(place == 2, inner, across))
    )
    bottom = jnp.where(
        place == 0, across, jnp.where(place == 1, inner, jnp.where(place == 2, half, outer_half))
    )
    neumann_two = jnp.concatenate([top, bottom], axis=0)
    return (interface_out[None, None], neumann_two[None, None])


def solution(mesh):
    return jax.shard_map(
        upward,
        mesh=mesh,
        in_specs=(
            P("box", None, None, None, "slab", None),
            P("box", None, None, None, "slab"),
            P("box", None, None, "slab"),
            P("box", None, None, "slab"),
            P("box", "slab", None, None),
            P("box", "slab", None, None),
        ),
        out_specs=(P("box", "slab", None, None), P("box", "slab", None, None)),
        check_vma=False,
    )
```
